32 devices in a mesh: tm: 8 (over y, x, core), row: 4 (over z).
Axes of the slice: x: 2, y: 2, z: 4, core: 2. Of those that a mesh axis runs over, the one named last changes fastest.
Arguments:
- section_maps: float32 [8, 1024, 1024], P('tm', 'row'), may hold values from -0.04375 to 1.09375, as said below
- terminal_cost: float32 [512, 512], P('row'), may hold values from -0.075 to 1.075, as said below
- terminal_states: float32 [512, 2048], replicated, may hold values from -6 to 6
Outputs:
- trajectories: float32 [8, 1024, 2048], P('tm', 'row')
- section_cost: float32 [8, 2048], P('tm', 'row')
The draws below stay inside these ranges and needn't reach their ends.
Inputs may be any that keep to these rules, and one draw needn't show every extreme that they name: `section_maps`: each section map is its diagonal plus small entries off the diagonal. `terminal_cost`: symmetric.
All inputs are finite; a program needn't handle non-finite values.
Results may differ from the reference program's by a relative error of at most 0.0003.
Values sent between devices are 32-bit elements; how exact they have to be, the bound alone decides.
No kernel may reach another device: no remote copies, remote signals or barrier semaphores. Data moves between devices by JAX's collectives and lax.ppermute only.
A program may use at most 64 MiB of HBM per device.

```python
import jax
import jax.numpy as jnp
from jax import lax

N_STATE = 512
TRAJ = 2048
HORIZON = 8


def draw_section_maps(key, part):
    noise_key = jax.random.fold_in(key, 11)
    diag_key = jax.random.fold_in(key, 12)
    wide = 2 * N_STATE
    noise = jax.random.truncated_normal(noise_key, -4.0, 4.0, (HORIZON, wide, wide), jnp.float32)
    diagonal = jax.random.uniform(diag_key, (HORIZON, wide, 1), jnp.float32, 0.8, 1.05)
    rows_id = lax.broadcasted_iota(jnp.int32, (wide, wide), 0)
    cols_id = lax.broadcasted_iota(jnp.int32, (wide, wide), 1)
    identity = (rows_id == cols_id).astype(jnp.float32)
    return 0.35 * noise / jnp.sqrt(jnp.float32(wide)) + diagonal * identity[None]


def draw_terminal_cost(key, part):
    noise_key = jax.random.fold_in(key, 21)
    diag_key = jax.random.fold_in(key, 22)
    noise = jax.random.truncated_normal(noise_key, -4.0, 4.0, (N_STATE, N_STATE), jnp.float32)
    levels_log = jax.random.uniform(diag_key, (N_STATE, 1), jnp.float32, jnp.log(0.3), 0.0)
    rows_id = lax.broadcasted_iota(jnp.int32, (N_STATE, N_STATE), 0)
    cols_id = lax.broadcasted_iota(jnp.int32, (N_STATE, N_STATE), 1)
    identity = (rows_id == cols_id).astype(jnp.float32)
    symmetric = 0.3 * (noise + jnp.transpose(noise)) / jnp.sqrt(jnp.float32(2 * N_STATE))
    return symmetric + jnp.exp(levels_log) * identity


def centred(key, dims, deviation, bound, kind=jnp.bfloat16):
    array = deviation * jax.random.normal(key, dims, jnp.float32)
    return jnp.clip(array, min=-bound, max=bound).astype(kind)


def setup_inputs(seed: int = 0) -> dict:
    streams_of = jax.random.split(jax.random.key(seed), 4)
    return {
        "section_maps": draw_section_maps(jax.random.fold_in(streams_of[3], 71), 0),
        "terminal_cost": draw_terminal_cost(jax.random.fold_in(streams_of[3], 71), 0),
        "terminal_states": centred(streams_of[2], (N_STATE, TRAJ), 1.0, 6.0, jnp.float32),
    }


def reference(section_maps, terminal_cost, terminal_states):
    state_dim = terminal_cost.shape[0]
    identity = jnp.eye(state_dim, dtype=jnp.float32)
    terminal_map = jnp.concatenate([identity, terminal_cost], axis=0)

    def advance_one(carried, section_map):
        composed = jnp.dot(section_map, carried, precision=lax.Precision.HIGHEST, preferred_element_type=jnp.float32)
        trajectory = jnp.dot(composed, terminal_states, precision=lax.Precision.HIGHEST, preferred_element_type=jnp.float32)
        return composed, trajectory

    unused_map, trajectories = lax.scan(advance_one, terminal_map, section_maps, reverse=True)
    section_cost = jnp.sum(trajectories[:, :state_dim] * trajectories[:, state_dim:], axis=1) / state_dim
    return trajectories, section_cost
```

```python
import jax
import jax.numpy as jnp
from jax import lax
from jax.sharding import PartitionSpec as P

CHUNKS = 4
AXES = ("tm", "row")


def product(left, right):
    return jnp.dot(left, right, precision=lax.Precision.HIGHEST, preferred_element_type=jnp.float32)


def assemble(pieces, place, count):
    ordered = []
    for q in range(count):
        picked = pieces[0]
        for d in range(1, count):
            picked = jnp.where((place - d) % count == q, pieces[d], picked)
        ordered.append(picked)
    return jnp.concatenate(ordered, axis=0)


def spread(block, source, target, count, with_self):
    pieces = [block] if with_self else []
    for d in range(0 if not with_self else 1, count):
        pairs = [(source * count + q, target * count + (q + d) % count) for q in range(count)]
        pieces.append(lax.ppermute(block, AXES, pairs))
    return pieces


def body(section_maps, terminal_cost, terminal_states):
    groups = lax.axis_size("tm")
    count = lax.axis_size("row")
    group = lax.axis_index("tm")
    place = lax.axis_index("row")
    local = section_maps[0]
    state_dim = local.shape[1] // 2
    width = state_dim // CHUNKS

    cost_rows = assemble(spread(terminal_cost, groups - 1, groups - 1, count, True), place, count)
    identity = jnp.eye(state_dim, dtype=jnp.float32)
    terminal_map = jnp.concatenate([identity, cost_rows], axis=0)
    incoming = [terminal_map[:, j * width:(j + 1) * width] for j in range(CHUNKS)]
    own = [None] * CHUNKS
    whole_first = [None] * CHUNKS
    for k in range(groups - 1, -1, -1):
        for j in range(CHUNKS):
            fresh = product(local, incoming[j])
            own[j] = fresh if own[j] is None else jnp.where(group == k, fresh, own[j])
            if k > 0:
                got = assemble(spread(fresh, k, k - 1, count, False), place, count)
                incoming[j] = jnp.where(group == k - 1, got, incoming[j])
            else:
                whole_first[j] = assemble(spread(fresh, 0, 0, count, True), place, count)
    own_rows = jnp.concatenate(own, axis=1)
    rows_traj = product(own_rows, terminal_states)

    cols = terminal_states.shape[1] // count
    my_cols = lax.dynamic_slice_in_dim(terminal_states, place * cols, cols, 1)

    def cost_of(whole):
        traj_cols = product(whole, my_cols)
        return jnp.sum(traj_cols[:state_dim] * traj_cols[state_dim:], axis=0) / state_dim

    next_whole = jnp.concatenate(incoming, axis=1)
    next_cost = cost_of(next_whole)
    back = lax.ppermute(next_cost, "tm", [(g, g + 1) for g in range(groups - 1)])
    first_cost = cost_of(jnp.concatenate(whole_first, axis=1))
    section_cost = jnp.where(group == 0, first_cost, back)
    return (rows_traj[None], section_cost[None])


def solution(mesh):
    in_specs = (P("tm", "row", None), P("row", None), P())
    out_specs = (P("tm", "row", None), P("tm", "row"))
    return jax.shard_map(body, mesh=mesh, in_specs=in_specs, out_specs=out_specs, check_vma=False)
```

```python
import jax
import jax.numpy as jnp
from jax import lax
from jax.sharding import PartitionSpec as P


def product(left, right):
    return jnp.dot(left, right, precision=lax.Precision.HIGHEST, preferred_element_type=jnp.float32)


def body(section_maps, terminal_cost, terminal_states):
    groups = lax.axis_size("tm")
    count = lax.axis_size("row")
    group = lax.axis_index("tm")
    place = lax.axis_index("row")
    state_dim = terminal_cost.shape[1]
    width = state_dim // count

    whole_map = lax.all_gather(section_maps[0], "row", axis=0, tiled=True)
    rows_id = lax.broadcasted_iota(jnp.int32, (state_dim, width), 0)
    cols_id = lax.broadcasted_iota(jnp.int32, (state_dim, width), 1) + place * width
    identity_cols = (rows_id == cols_id).astype(jnp.float32)
    incoming = jnp.concatenate([identity_cols, terminal_cost.T], axis=0)

    own = None
    for k in range(groups - 1, -1, -1):
        fresh = product(whole_map, incoming)
        own = fresh if own is None else jnp.where(group == k, fresh, own)
        if k > 0:
            got = lax.ppermute(fresh, "tm", [(k, k - 1)])
            incoming = jnp.where(group == k - 1, got, incoming)

    value_map = lax.all_gather(own, "row", axis=1, tiled=True)
    rows = value_map.shape[0] // count
    my_rows = lax.dynamic_slice_in_dim(value_map, place * rows, rows, 0)
    rows_traj = product(my_rows, terminal_states)

    cols = terminal_states.shape[1] // count
    my_cols = lax.dynamic_slice_in_dim(terminal_states, place * cols, cols, 1)
    traj_cols = product(value_map, my_cols)
    section_cost = jnp.sum(traj_cols[:state_dim] * traj_cols[state_dim:], axis=0) / state_dim
    return (rows_traj[None], section_cost[None])


def solution(mesh):
    in_specs = (P("tm", "row", None), P("row", None), P())
    out_specs = (P("tm", "row", None), P("tm", "row"))
    return jax.shard_map(body, mesh=mesh, in_specs=in_specs, out_specs=out_specs, check_vma=False)
```

```python
import jax
import jax.numpy as jnp
from jax import lax
from jax.sharding import PartitionSpec as P


def product(left, right):
    return jnp.dot(left, right, precision=lax.Precision.HIGH, preferred_element_type=jnp.float32)


def body(section_maps, terminal_cost, terminal_states):
    groups = lax.axis_size("tm")
    count = lax.axis_size("row")
    group = lax.axis_index("tm")
    place = lax.axis_index("row")
    state_dim = terminal_cost.shape[1]
    width = state_dim // count

    whole_map = lax.all_gather(section_maps[0], "row", axis=0, tiled=True)
    rows_id = lax.broadcasted_iota(jnp.int32, (state_dim, width), 0)
    cols_id = lax.broadcasted_iota(jnp.int32, (state_dim, width), 1) + place * width
    identity_cols = (rows_id == cols_id).astype(jnp.float32)
    incoming = jnp.concatenate([identity_cols, terminal_cost.T], axis=0)

    own = None
    for k in range(groups - 1, -1, -1):
        fresh = product(whole_map, incoming)
        own = fresh if own is None else jnp.where(group == k, fresh, own)
        if k > 0:
            got = lax.ppermute(fresh, "tm", [(k, k - 1)])
            incoming = jnp.where(group == k - 1, got, incoming)

    value_map = lax.all_gather(own, "row", axis=1, tiled=True)
    rows = value_map.shape[0] // count
    my_rows = lax.dynamic_slice_in_dim(value_map, place * rows, rows, 0)
    rows_traj = product(my_rows, terminal_states)

    cols = terminal_states.shape[1] // count
    my_cols = lax.dynamic_slice_in_dim(terminal_states, place * cols, cols, 1)
    traj_cols = product(value_map, my_cols)
    section_cost = jnp.sum(traj_cols[:state_dim] * traj_cols[state_dim:], axis=0) / state_dim
    return (rows_traj[None], section_cost[None])


def solution(mesh):
    in_specs = (P("tm", "row", None), P("row", None), P())
    out_specs = (P("tm", "row", None), P("tm", "row"))
    return jax.shard_map(body, mesh=mesh, in_specs=in_specs, out_specs=out_specs, check_vma=False)
```

```python
import jax
import jax.numpy as jnp
from jax import lax
from jax.sharding import PartitionSpec as P


def split(values):
    high = values.astype(jnp.bfloat16)
    low = (values - high.astype(jnp.float32)).astype(jnp.bfloat16)
    return high, low


def left_of(values):
    high, low = split(values)
    return jnp.concatenate([high, high, low], axis=1)


def right_of(values):
    high, low = split(values)
    return jnp.concatenate([high, low, high], axis=0)


def product3(left3, right3):
    return jnp.dot(left3, right3, preferred_element_type=jnp.float32)


def body(section_maps, terminal_cost, terminal_states):
    groups = lax.axis_size("tm")
    count = lax.axis_size("row")
    group = lax.axis_index("tm")
    place = lax.axis_index("row")
    state_dim = terminal_cost.shape[1]
    width = state_dim // count

    whole_map = lax.all_gather(section_maps[0], "row", axis=0, tiled=True)
    map3 = left_of(whole_map)
    rows_id = lax.broadcasted_iota(jnp.int32, (state_dim, width), 0)
    cols_id = lax.broadcasted_iota(jnp.int32, (state_dim, width), 1) + place * width
    identity_cols = (rows_id == cols_id).astype(jnp.float32)
    incoming = jnp.concatenate([identity_cols, terminal_cost.T], axis=0)

    own = None
    for k in range(groups - 1, -1, -1):
        fresh = product3(map3, right_of(incoming))
        own = fresh if own is None else jnp.where(group == k, fresh, own)
        if k > 0:
            got = lax.ppermute(fresh, "tm", [(k, k - 1)])
            incoming = jnp.where(group == k - 1, got, incoming)

    value_map = lax.all_gather(own, "row", axis=1, tiled=True)
    rows = value_map.shape[0] // count
    my_rows = lax.dynamic_slice_in_dim(value_map, place * rows, rows, 0)
    rows_traj = product3(left_of(my_rows), right_of(terminal_states))

    cols = terminal_states.shape[1] // count
    my_cols = lax.dynamic_slice_in_dim(terminal_states, place * cols, cols, 1)
    traj_cols = product3(left_of(value_map), right_of(my_cols))
    section_cost = jnp.sum(traj_cols[:state_dim] * traj_cols[state_dim:], axis=0) / state_dim
    return (rows_traj[None], section_cost[None])


def solution(mesh):
    in_specs = (P("tm", "row", None), P("row", None), P())
    out_specs = (P("tm", "row", None), P("tm", "row"))
    return jax.shard_map(body, mesh=mesh, in_specs=in_specs, out_specs=out_specs, check_vma=False)
```

```python
import jax
import jax.numpy as jnp
from jax import lax
from jax.sharding import PartitionSpec as P

CHUNKS = 2


def product(left, right):
    return jnp.dot(left, right, precision=lax.Precision.HIGH, preferred_element_type=jnp.float32)


def body(section_maps, terminal_cost, terminal_states):
    groups = lax.axis_size("tm")
    count = lax.axis_size("row")
    group = lax.axis_index("tm")
    place = lax.axis_index("row")
    state_dim = terminal_cost.shape[1]
    width = state_dim // count

    whole_map = lax.all_gather(section_maps[0], "row", axis=0, tiled=True)
    rows_id = lax.broadcasted_iota(jnp.int32, (state_dim, width), 0)
    cols_id = lax.broadcasted_iota(jnp.int32, (state_dim, width), 1) + place * width
    identity_cols = (rows_id == cols_id).astype(jnp.float32)
    incoming = jnp.concatenate([identity_cols, terminal_cost.T], axis=0)

    step = width // CHUNKS
    incoming = [incoming[:, j * step:(j + 1) * step] for j in range(CHUNKS)]
    own = [None] * CHUNKS
    for k in range(groups - 1, -1, -1):
        for j in range(CHUNKS):
            fresh = product(whole_map, incoming[j])
            own[j] = fresh if own[j] is None else jnp.where(group == k, fresh, own[j])
            if k > 0:
                got = lax.ppermute(fresh, "tm", [(k, k - 1)])
                incoming[j] = jnp.where(group == k - 1, got, incoming[j])

    value_map = lax.all_gather(jnp.concatenate(own, axis=1), "row", axis=1, tiled=True)
    rows = value_map.shape[0] // count
    my_rows = lax.dynamic_slice_in_dim(value_map, place * rows, rows, 0)
    rows_traj = product(my_rows, terminal_states)

    cols = terminal_states.shape[1] // count
    my_cols = lax.dynamic_slice_in_dim(terminal_states, place * cols, cols, 1)
    traj_cols = product(value_map, my_cols)
    section_cost = jnp.sum(traj_cols[:state_dim] * traj_cols[state_dim:], axis=0) / state_dim
    return (rows_traj[None], section_cost[None])


def solution(mesh):
    in_specs = (P("tm", "row", None), P("row", None), P())
    out_specs = (P("tm", "row", None), P("tm", "row"))
    return jax.shard_map(body, mesh=mesh, in_specs=in_specs, out_specs=out_specs, check_vma=False)
```

```python
import jax
import jax.numpy as jnp
from jax import lax
from jax.sharding import PartitionSpec as P

CHUNKS = 2


def product(left, right):
    return jnp.dot(left, right, precision=lax.Precision.HIGH, preferred_element_type=jnp.float32)


def body(section_maps, terminal_cost, terminal_states):
    groups = lax.axis_size("tm")
    count = lax.axis_size("row")
    group = lax.axis_index("tm")
    place = lax.axis_index("row")
    state_dim = terminal_cost.shape[1]
    width = state_dim // count

    whole_map = lax.all_gather(section_maps[0], "row", axis=0, tiled=True)
    rows_id = lax.broadcasted_iota(jnp.int32, (state_dim, width), 0)
    cols_id = lax.broadcasted_iota(jnp.int32, (state_dim, width), 1) + place * width
    identity_cols = (rows_id == cols_id).astype(jnp.float32)
    incoming = jnp.concatenate([identity_cols, terminal_cost.T], axis=0)

    step = width // CHUNKS
    incoming = [incoming[:, j * step:(j + 1) * step] for j in range(CHUNKS)]
    own = [None] * CHUNKS
    for k in range(groups - 1, -1, -1):
        for j in range(CHUNKS):
            fresh = lax.cond(group == k, product, lambda a, b: jnp.zeros((a.shape[0], b.shape[1]), jnp.float32),
                             whole_map, incoming[j])
            own[j] = fresh if own[j] is None else jnp.where(group == k, fresh, own[j])
            if k > 0:
                got = lax.ppermute(fresh, "tm", [(k, k - 1)])
                incoming[j] = jnp.where(group == k - 1, got, incoming[j])

    value_map = lax.all_gather(jnp.concatenate(own, axis=1), "row", axis=1, tiled=True)
    rows = value_map.shape[0] // count
    my_rows = lax.dynamic_slice_in_dim(value_map, place * rows, rows, 0)
    rows_traj = product(my_rows, terminal_states)

    cols = terminal_states.shape[1] // count
    my_cols = lax.dynamic_slice_in_dim(terminal_states, place * cols, cols, 1)
    traj_cols = product(value_map, my_cols)
    section_cost = jnp.sum(traj_cols[:state_dim] * traj_cols[state_dim:], axis=0) / state_dim
    return (rows_traj[None], section_cost[None])


def solution(mesh):
    in_specs = (P("tm", "row", None), P("row", None), P())
    out_specs = (P("tm", "row", None), P("tm", "row"))
    return jax.shard_map(body, mesh=mesh, in_specs=in_specs, out_specs=out_specs, check_vma=False)
```

```python
import jax
import jax.numpy as jnp
from jax import lax
from jax.sharding import PartitionSpec as P

CHUNKS = 2


def product(left, right):
    return jnp.dot(left, right, precision=lax.Precision.HIGH, preferred_element_type=jnp.float32)


def body(section_maps, terminal_cost, terminal_states):
    groups = lax.axis_size("tm")
    count = lax.axis_size("row")
    group = lax.axis_index("tm")
    place = lax.axis_index("row")
    state_dim = terminal_cost.shape[1]
    width = state_dim // count

    whole_map = lax.all_gather(section_maps[0], "row", axis=0, tiled=True)
    rows_id = lax.broadcasted_iota(jnp.int32, (state_dim, width), 0)
    cols_id = lax.broadcasted_iota(jnp.int32, (state_dim, width), 1) + place * width
    identity_cols = (rows_id == cols_id).astype(jnp.float32)
    incoming = jnp.concatenate([identity_cols, terminal_cost.T], axis=0)

    step = width // CHUNKS
    incoming = [incoming[:, j * step:(j + 1) * step] for j in range(CHUNKS)]
    own = [None] * CHUNKS
    for k in range(groups - 1, -1, -1):
        for j in range(CHUNKS):
            fresh = product(whole_map, incoming[j])
            own[j] = fresh if own[j] is None else jnp.where(group == k, fresh, own[j])
            if k > 0:
                got = lax.ppermute(fresh, "tm", [(k, k - 1)])
                incoming[j] = jnp.where(group == k - 1, got, incoming[j])

    own_cols = jnp.concatenate(own, axis=1)
    rows = own_cols.shape[0] // count
    half = count // 2
    blocks = own_cols.reshape(count, rows, width)
    main_pieces = [blocks[place]]
    pair_pieces = [blocks[(place + half) % count]]
    for d in range(1, count):
        target = (place + d) % count
        payload = jnp.concatenate([blocks[target], blocks[(target + half) % count]], axis=0)
        got = lax.ppermute(payload, "row", [(z, (z + d) % count) for z in range(count)])
        main_pieces.append(got[:rows])
        pair_pieces.append(got[rows:])

    def in_order(pieces):
        ordered = []
        for q in range(count):
            picked = pieces[0]
            for d in range(1, count):
                picked = jnp.where((place - d) % count == q, pieces[d], picked)
            ordered.append(picked)
        return jnp.concatenate(ordered, axis=1)

    rows_traj = product(in_order(main_pieces), terminal_states)
    pair_traj = product(in_order(pair_pieces), terminal_states)
    partial = jnp.sum(rows_traj * pair_traj, axis=0)
    cols = terminal_states.shape[1] // count
    total = lax.dynamic_slice_in_dim(partial, place * cols, cols, 0)
    for e in range(1, half):
        target = (place + e) % count
        sent = lax.dynamic_slice_in_dim(partial, target * cols, cols, 0)
        total = total + lax.ppermute(sent, "row", [(z, (z + e) % count) for z in range(count)])
    section_cost = total / state_dim
    return (rows_traj[None], section_cost[None])


def solution(mesh):
    in_specs = (P("tm", "row", None), P("row", None), P())
    out_specs = (P("tm", "row", None), P("tm", "row"))
    return jax.shard_map(body, mesh=mesh, in_specs=in_specs, out_specs=out_specs, check_vma=False)
```

```python
import jax
import jax.numpy as jnp
from jax import lax
from jax.sharding import PartitionSpec as P

CHUNKS = 2


def product(left, right):
    return jnp.dot(left, right, precision=lax.Precision.HIGH, preferred_element_type=jnp.float32)


def split(values):
    high = values.astype(jnp.bfloat16)
    low = (values - high.astype(jnp.float32)).astype(jnp.bfloat16)
    return high, low


def left_of(values):
    high, low = split(values)
    return jnp.concatenate([high, high, low], axis=1)


def right_of(values):
    high, low = split(values)
    return jnp.concatenate([high, low, high], axis=0)


def product3(left3, right3):
    return jnp.dot(left3, right3, preferred_element_type=jnp.float32)


def step_of(map3, block):
    return product3(map3, right_of(block))


def idle_of(map3, block):
    return jnp.zeros((map3.shape[0], block.shape[1]), jnp.float32)


def body(section_maps, terminal_cost, terminal_states):
    groups = lax.axis_size("tm")
    count = lax.axis_size("row")
    group = lax.axis_index("tm")
    place = lax.axis_index("row")
    state_dim = terminal_cost.shape[1]
    width = state_dim // count

    whole_map = lax.all_gather(section_maps[0], "row", axis=0, tiled=True)
    map3 = left_of(whole_map)
    states3 = right_of(terminal_states)
    rows_id = lax.broadcasted_iota(jnp.int32, (state_dim, width), 0)
    cols_id = lax.broadcasted_iota(jnp.int32, (state_dim, width), 1) + place * width
    identity_cols = (rows_id == cols_id).astype(jnp.float32)
    incoming = jnp.concatenate([identity_cols, terminal_cost.T], axis=0)

    step = width // CHUNKS
    incoming = [incoming[:, j * step:(j + 1) * step] for j in range(CHUNKS)]
    own = [None] * CHUNKS
    for k in range(groups - 1, -1, -1):
        for j in range(CHUNKS):
            fresh = lax.cond(group == k, step_of, idle_of, map3, incoming[j])
            own[j] = fresh if own[j] is None else jnp.where(group == k, fresh, own[j])
            if k > 0:
                got = lax.ppermute(fresh, "tm", [(k, k - 1)])
                incoming[j] = jnp.where(group == k - 1, got, incoming[j])

    own_cols = jnp.concatenate(own, axis=1)
    rows = own_cols.shape[0] // count
    half = count // 2
    blocks = own_cols.reshape(count, rows, width)
    main_pieces = [blocks[place]]
    pair_pieces = [blocks[(place + half) % count]]
    for d in range(1, count):
        target = (place + d) % count
        payload = jnp.concatenate([blocks[target], blocks[(target + half) % count]], axis=0)
        got = lax.ppermute(payload, "row", [(z, (z + d) % count) for z in range(count)])
        main_pieces.append(got[:rows])
        pair_pieces.append(got[rows:])

    def in_order(pieces):
        ordered = []
        for q in range(count):
            picked = pieces[0]
            for d in range(1, count):
                picked = jnp.where((place - d) % count == q, pieces[d], picked)
            ordered.append(picked)
        return jnp.concatenate(ordered, axis=1)

    rows_traj = product3(left_of(in_order(main_pieces)), states3)
    pair_traj = product3(left_of(in_order(pair_pieces)), states3)
    partial = jnp.sum(rows_traj * pair_traj, axis=0)
    cols = terminal_states.shape[1] // count
    total = lax.dynamic_slice_in_dim(partial, place * cols, cols, 0)
    for e in range(1, half):
        target = (place + e) % count
        sent = lax.dynamic_slice_in_dim(partial, target * cols, cols, 0)
        total = total + lax.ppermute(sent, "row", [(z, (z + e) % count) for z in range(count)])
    section_cost = total / state_dim
    return (rows_traj[None], section_cost[None])


def solution(mesh):
    in_specs = (P("tm", "row", None), P("row", None), P())
    out_specs = (P("tm", "row", None), P("tm", "row"))
    return jax.shard_map(body, mesh=mesh, in_specs=in_specs, out_specs=out_specs, check_vma=False)
```

```python
import jax
import jax.numpy as jnp
from jax import lax
from jax.sharding import PartitionSpec as P

CHUNKS = 2


def product(left, right):
    return jnp.dot(left, right, precision=lax.Precision.HIGH, preferred_element_type=jnp.float32)


def line_gather(block, place, count):
    rightward = block
    leftward = block
    from_left = []
    from_right = []
    for t in range(1, count):
        rightward = lax.ppermute(rightward, "row", [(z, z + 1) for z in range(t - 1, count - 1)])
        leftward = lax.ppermute(leftward, "row", [(z, z - 1) for z in range(1, count - t + 1)])
        from_left.append(rightward)
        from_right.append(leftward)
    by_offset = jnp.concatenate(from_left[::-1] + [block] + from_right, axis=0)
    rows = block.shape[0]
    return lax.dynamic_slice_in_dim(by_offset, (count - 1 - place) * rows, count * rows, 0)


def body(section_maps, terminal_cost, terminal_states):
    groups = lax.axis_size("tm")
    count = lax.axis_size("row")
    group = lax.axis_index("tm")
    place = lax.axis_index("row")
    state_dim = terminal_cost.shape[1]
    width = state_dim // count

    whole_map = line_gather(section_maps[0], place, count)
    rows_id = lax.broadcasted_iota(jnp.int32, (state_dim, width), 0)
    cols_id = lax.broadcasted_iota(jnp.int32, (state_dim, width), 1) + place * width
    identity_cols = (rows_id == cols_id).astype(jnp.float32)
    incoming = jnp.concatenate([identity_cols, terminal_cost.T], axis=0)

    step = width // CHUNKS
    incoming = [incoming[:, j * step:(j + 1) * step] for j in range(CHUNKS)]
    own = [None] * CHUNKS
    for k in range(groups - 1, -1, -1):
        for j in range(CHUNKS):
            fresh = product(whole_map, incoming[j])
            own[j] = fresh if own[j] is None else jnp.where(group == k, fresh, own[j])
            if k > 0:
                got = lax.ppermute(fresh, "tm", [(k, k - 1)])
                incoming[j] = jnp.where(group == k - 1, got, incoming[j])

    own_cols = jnp.concatenate(own, axis=1)
    rows = own_cols.shape[0] // count
    half = count // 2
    blocks = own_cols.reshape(count, rows, width)
    main_pieces = [blocks[place]]
    pair_pieces = [blocks[(place + half) % count]]
    for d in range(1, count):
        target = (place + d) % count
        payload = jnp.concatenate([blocks[target], blocks[(target + half) % count]], axis=0)
        got = lax.ppermute(payload, "row", [(z, (z + d) % count) for z in range(count)])
        main_pieces.append(got[:rows])
        pair_pieces.append(got[rows:])

    def in_order(pieces):
        ordered = []
        for q in range(count):
            picked = pieces[0]
            for d in range(1, count):
                picked = jnp.where((place - d) % count == q, pieces[d], picked)
            ordered.append(picked)
        return jnp.concatenate(ordered, axis=1)

    rows_traj = product(in_order(main_pieces), terminal_states)
    pair_traj = product(in_order(pair_pieces), terminal_states)
    partial = jnp.sum(rows_traj * pair_traj, axis=0)
    cols = terminal_states.shape[1] // count
    total = lax.dynamic_slice_in_dim(partial, place * cols, cols, 0)
    for e in range(1, half):
        target = (place + e) % count
        sent = lax.dynamic_slice_in_dim(partial, target * cols, cols, 0)
        total = total + lax.ppermute(sent, "row", [(z, (z + e) % count) for z in range(count)])
    section_cost = total / state_dim
    return (rows_traj[None], section_cost[None])


def solution(mesh):
    in_specs = (P("tm", "row", None), P("row", None), P())
    out_specs = (P("tm", "row", None), P("tm", "row"))
    return jax.shard_map(body, mesh=mesh, in_specs=in_specs, out_specs=out_specs, check_vma=False)
```

```python
import jax
import jax.numpy as jnp
from jax import lax
from jax.sharding import PartitionSpec as P

CHUNKS = 2


def product(left, right):
    return jnp.dot(left, right, precision=lax.Precision.HIGH, preferred_element_type=jnp.float32)


def line_gather(block, place, count):
    rightward = block
    leftward = block
    from_left = []
    from_right = []
    for t in range(1, count):
        rightward = lax.ppermute(rightward, "row", [(z, z + 1) for z in range(t - 1, count - 1)])
        leftward = lax.ppermute(leftward, "row", [(z, z - 1) for z in range(1, count - t + 1)])
        from_left.append(rightward)
        from_right.append(leftward)
    by_offset = jnp.concatenate(from_left[::-1] + [block] + from_right, axis=0)
    rows = block.shape[0]
    return lax.dynamic_slice_in_dim(by_offset, (count - 1 - place) * rows, count * rows, 0)


def body(section_maps, terminal_cost, terminal_states):
    groups = lax.axis_size("tm")
    count = lax.axis_size("row")
    group = lax.axis_index("tm")
    place = lax.axis_index("row")
    state_dim = terminal_cost.shape[1]
    width = state_dim // count

    whole_map = lax.optimization_barrier(line_gather(section_maps[0], place, count))
    rows_id = lax.broadcasted_iota(jnp.int32, (state_dim, width), 0)
    cols_id = lax.broadcasted_iota(jnp.int32, (state_dim, width), 1) + place * width
    identity_cols = (rows_id == cols_id).astype(jnp.float32)
    incoming = jnp.concatenate([identity_cols, terminal_cost.T], axis=0)

    step = width // CHUNKS
    incoming = [incoming[:, j * step:(j + 1) * step] for j in range(CHUNKS)]
    own = [None] * CHUNKS
    for k in range(groups - 1, -1, -1):
        for j in range(CHUNKS):
            fresh = product(whole_map, incoming[j])
            own[j] = fresh if own[j] is None else jnp.where(group == k, fresh, own[j])
            if k > 0:
                got = lax.ppermute(fresh, "tm", [(k, k - 1)])
                incoming[j] = jnp.where(group == k - 1, got, incoming[j])

    own_cols = jnp.concatenate(own, axis=1)
    rows = own_cols.shape[0] // count
    half = count // 2
    blocks = own_cols.reshape(count, rows, width)
    main_pieces = [blocks[place]]
    pair_pieces = [blocks[(place + half) % count]]
    for d in range(1, count):
        target = (place + d) % count
        payload = jnp.concatenate([blocks[target], blocks[(target + half) % count]], axis=0)
        got = lax.ppermute(payload, "row", [(z, (z + d) % count) for z in range(count)])
        main_pieces.append(got[:rows])
        pair_pieces.append(got[rows:])

    def in_order(pieces):
        ordered = []
        for q in range(count):
            picked = pieces[0]
            for d in range(1, count):
                picked = jnp.where((place - d) % count == q, pieces[d], picked)
            ordered.append(picked)
        return jnp.concatenate(ordered, axis=1)

    rows_traj = product(in_order(main_pieces), terminal_states)
    pair_traj = product(in_order(pair_pieces), terminal_states)
    partial = jnp.sum(rows_traj * pair_traj, axis=0)
    cols = terminal_states.shape[1] // count
    total = lax.dynamic_slice_in_dim(partial, place * cols, cols, 0)
    for e in range(1, half):
        target = (place + e) % count
        sent = lax.dynamic_slice_in_dim(partial, target * cols, cols, 0)
        total = total + lax.ppermute(sent, "row", [(z, (z + e) % count) for z in range(count)])
    section_cost = total / state_dim
    return (rows_traj[None], section_cost[None])


def solution(mesh):
    in_specs = (P("tm", "row", None), P("row", None), P())
    out_specs = (P("tm", "row", None), P("tm", "row"))
    return jax.shard_map(body, mesh=mesh, in_specs=in_specs, out_specs=out_specs, check_vma=False)
```

```python
import jax
import jax.numpy as jnp
from jax import lax
from jax.sharding import PartitionSpec as P

CHUNKS = 2


def product(left, right):
    return jnp.dot(left, right, precision=lax.Precision.HIGH, preferred_element_type=jnp.float32)


def line_gather(block, place, count):
    rightward = block
    leftward = block
    from_left = []
    from_right = []
    for t in range(1, count):
        rightward = lax.ppermute(rightward, "row", [(z, z + 1) for z in range(t - 1, count - 1)])
        leftward = lax.ppermute(leftward, "row", [(z, z - 1) for z in range(1, count - t + 1)])
        from_left.append(rightward)
        from_right.append(leftward)
    by_offset = jnp.concatenate(from_left[::-1] + [block] + from_right, axis=0)
    rows = block.shape[0]
    return lax.dynamic_slice_in_dim(by_offset, (count - 1 - place) * rows, count * rows, 0)


def body(section_maps, terminal_cost, terminal_states):
    groups = lax.axis_size("tm")
    count = lax.axis_size("row")
    group = lax.axis_index("tm")
    place = lax.axis_index("row")
    state_dim = terminal_cost.shape[1]
    width = state_dim // count

    local = section_maps[0]
    cut = local.shape[0] // 2
    upper = line_gather(local[:cut], place, count).reshape(count, cut, local.shape[1])
    lower = line_gather(local[cut:], place, count).reshape(count, cut, local.shape[1])
    whole_map = jnp.concatenate([upper, lower], axis=1).reshape(count * local.shape[0], local.shape[1])
    whole_map = lax.optimization_barrier(whole_map)
    rows_id = lax.broadcasted_iota(jnp.int32, (state_dim, width), 0)
    cols_id = lax.broadcasted_iota(jnp.int32, (state_dim, width), 1) + place * width
    identity_cols = (rows_id == cols_id).astype(jnp.float32)
    incoming = jnp.concatenate([identity_cols, terminal_cost.T], axis=0)

    step = width // CHUNKS
    incoming = [incoming[:, j * step:(j + 1) * step] for j in range(CHUNKS)]
    own = [None] * CHUNKS
    for k in range(groups - 1, -1, -1):
        for j in range(CHUNKS):
            fresh = product(whole_map, incoming[j])
            own[j] = fresh if own[j] is None else jnp.where(group == k, fresh, own[j])
            if k > 0:
                got = lax.ppermute(fresh, "tm", [(k, k - 1)])
                incoming[j] = jnp.where(group == k - 1, got, incoming[j])

    own_cols = jnp.concatenate(own, axis=1)
    rows = own_cols.shape[0] // count
    half = count // 2
    blocks = own_cols.reshape(count, rows, width)
    main_pieces = [blocks[place]]
    pair_pieces = [blocks[(place + half) % count]]
    for d in range(1, count):
        target = (place + d) % count
        payload = jnp.concatenate([blocks[target], blocks[(target + half) % count]], axis=0)
        got = lax.ppermute(payload, "row", [(z, (z + d) % count) for z in range(count)])
        main_pieces.append(got[:rows])
        pair_pieces.append(got[rows:])

    def in_order(pieces):
        ordered = []
        for q in range(count):
            picked = pieces[0]
            for d in range(1, count):
                picked = jnp.where((place - d) % count == q, pieces[d], picked)
            ordered.append(picked)
        return jnp.concatenate(ordered, axis=1)

    rows_traj = product(in_order(main_pieces), terminal_states)
    pair_traj = product(in_order(pair_pieces), terminal_states)
    partial = jnp.sum(rows_traj * pair_traj, axis=0)
    cols = terminal_states.shape[1] // count
    total = lax.dynamic_slice_in_dim(partial, place * cols, cols, 0)
    if half == 2:
        partner = [(z, z ^ 1) for z in range(count)]
        sent = lax.dynamic_slice_in_dim(partial, (place ^ 1) * cols, cols, 0)
        total = total + lax.ppermute(sent, "row", partner)
    else:
        for e in range(1, half):
            target = (place + e) % count
            sent = lax.dynamic_slice_in_dim(partial, target * cols, cols, 0)
            total = total + lax.ppermute(sent, "row", [(z, (z + e) % count) for z in range(count)])
    section_cost = total / state_dim
    return (rows_traj[None], section_cost[None])


def solution(mesh):
    in_specs = (P("tm", "row", None), P("row", None), P())
    out_specs = (P("tm", "row", None), P("tm", "row"))
    return jax.shard_map(body, mesh=mesh, in_specs=in_specs, out_specs=out_specs, check_vma=False)
```

```python
import jax
import jax.numpy as jnp
from jax import lax
from jax.sharding import PartitionSpec as P

CHUNKS = 2


def product(left, right):
    return jnp.dot(left, right, precision=lax.Precision.HIGH, preferred_element_type=jnp.float32)


def line_gather(block, place, count):
    rightward = block
    leftward = block
    from_left = []
    from_right = []
    for t in range(1, count):
        rightward = lax.ppermute(rightward, "row", [(z, z + 1) for z in range(t - 1, count - 1)])
        leftward = lax.ppermute(leftward, "row", [(z, z - 1) for z in range(1, count - t + 1)])
        from_left.append(rightward)
        from_right.append(leftward)
    by_offset = jnp.concatenate(from_left[::-1] + [block] + from_right, axis=0)
    rows = block.shape[0]
    return lax.dynamic_slice_in_dim(by_offset, (count - 1 - place) * rows, count * rows, 0)


def body(section_maps, terminal_cost, terminal_states):
    groups = lax.axis_size("tm")
    count = lax.axis_size("row")
    group = lax.axis_index("tm")
    place = lax.axis_index("row")
    state_dim = terminal_cost.shape[1]
    width = state_dim // count

    local = section_maps[0]
    cut = local.shape[0] // 2
    upper = line_gather(local[:cut], place, count).reshape(count, cut, local.shape[1])
    lower = line_gather(local[cut:], place, count).reshape(count, cut, local.shape[1])
    whole_map = jnp.concatenate([upper, lower], axis=1).reshape(count * local.shape[0], local.shape[1])
    whole_map = lax.optimization_barrier(whole_map)
    rows_id = lax.broadcasted_iota(jnp.int32, (state_dim, width), 0)
    cols_id = lax.broadcasted_iota(jnp.int32, (state_dim, width), 1) + place * width
    identity_cols = (rows_id == cols_id).astype(jnp.float32)
    incoming = jnp.concatenate([identity_cols, terminal_cost.T], axis=0)

    step = width // CHUNKS
    incoming = [incoming[:, j * step:(j + 1) * step] for j in range(CHUNKS)]
    own = [None] * CHUNKS
    for k in range(groups - 1, -1, -1):
        for j in range(CHUNKS):
            fresh = product(whole_map, incoming[j])
            own[j] = fresh if own[j] is None else jnp.where(group == k, fresh, own[j])
            if k > 0:
                got = lax.ppermute(fresh, "tm", [(k, k - 1)])
                incoming[j] = jnp.where(group == k - 1, got, incoming[j])

    own_cols = jnp.concatenate(own, axis=1)
    rows = own_cols.shape[0] // count
    half = count // 2
    blocks = own_cols.reshape(count, rows, width)
    main_pieces = [blocks[place]]
    pair_pieces = [blocks[(place + half) % count]]
    for d in range(1, count):
        target = (place + d) % count
        payload = jnp.concatenate([blocks[target], blocks[(target + half) % count]], axis=0)
        got = lax.ppermute(payload, "row", [(z, (z + d) % count) for z in range(count)])
        main_pieces.append(got[:rows])
        pair_pieces.append(got[rows:])

    def in_order(pieces):
        ordered = []
        for q in range(count):
            picked = pieces[0]
            for d in range(1, count):
                picked = jnp.where((place - d) % count == q, pieces[d], picked)
            ordered.append(picked)
        return jnp.concatenate(ordered, axis=1)

    main_rows = in_order(main_pieces)
    pair_rows = in_order(pair_pieces)
    cols = terminal_states.shape[1] // count

    def partial_for(target):
        states = lax.dynamic_slice_in_dim(terminal_states, target * cols, cols, 1)
        return jnp.sum(product(main_rows, states) * product(pair_rows, states), axis=0)

    if half == 2:
        sent = partial_for(place ^ 1)
        got = lax.ppermute(sent, "row", [(z, z ^ 1) for z in range(count)])
        rows_traj = product(main_rows, terminal_states)
        total = partial_for(place) + got
    else:
        rows_traj = product(main_rows, terminal_states)
        total = partial_for(place)
        for e in range(1, half):
            target = (place + e) % count
            total = total + lax.ppermute(partial_for(target), "row", [(z, (z + e) % count) for z in range(count)])
    section_cost = total / state_dim
    return (rows_traj[None], section_cost[None])


def solution(mesh):
    in_specs = (P("tm", "row", None), P("row", None), P())
    out_specs = (P("tm", "row", None), P("tm", "row"))
    return jax.shard_map(body, mesh=mesh, in_specs=in_specs, out_specs=out_specs, check_vma=False)
```

```python
import jax
import jax.numpy as jnp
from jax import lax
from jax.sharding import PartitionSpec as P

CHUNKS = 2
GATHER_PARTS = 4


def product(left, right):
    return jnp.dot(left, right, precision=lax.Precision.HIGH, preferred_element_type=jnp.float32)


def line_gather(block, place, count):
    rightward = block
    leftward = block
    from_left = []
    from_right = []
    for t in range(1, count):
        rightward = lax.ppermute(rightward, "row", [(z, z + 1) for z in range(t - 1, count - 1)])
        leftward = lax.ppermute(leftward, "row", [(z, z - 1) for z in range(1, count - t + 1)])
        from_left.append(rightward)
        from_right.append(leftward)
    by_offset = jnp.concatenate(from_left[::-1] + [block] + from_right, axis=0)
    rows = block.shape[0]
    return lax.dynamic_slice_in_dim(by_offset, (count - 1 - place) * rows, count * rows, 0)


def body(section_maps, terminal_cost, terminal_states):
    groups = lax.axis_size("tm")
    count = lax.axis_size("row")
    group = lax.axis_index("tm")
    place = lax.axis_index("row")
    state_dim = terminal_cost.shape[1]
    width = state_dim // count

    local = section_maps[0]
    cut = local.shape[0] // GATHER_PARTS
    parts = [line_gather(local[p * cut:(p + 1) * cut], place, count).reshape(count, cut, local.shape[1])
             for p in range(GATHER_PARTS)]
    whole_map = jnp.concatenate(parts, axis=1).reshape(count * local.shape[0], local.shape[1])
    whole_map = lax.optimization_barrier(whole_map)
    rows_id = lax.broadcasted_iota(jnp.int32, (state_dim, width), 0)
    cols_id = lax.broadcasted_iota(jnp.int32, (state_dim, width), 1) + place * width
    identity_cols = (rows_id == cols_id).astype(jnp.float32)
    incoming = jnp.concatenate([identity_cols, terminal_cost.T], axis=0)

    step = width // CHUNKS
    incoming = [incoming[:, j * step:(j + 1) * step] for j in range(CHUNKS)]
    own = [None] * CHUNKS
    for k in range(groups - 1, -1, -1):
        for j in range(CHUNKS):
            fresh = product(whole_map, incoming[j])
            own[j] = fresh if own[j] is None else jnp.where(group == k, fresh, own[j])
            if k > 0:
                got = lax.ppermute(fresh, "tm", [(k, k - 1)])
                incoming[j] = jnp.where(group == k - 1, got, incoming[j])

    own_cols = jnp.concatenate(own, axis=1)
    rows = own_cols.shape[0] // count
    half = count // 2
    blocks = own_cols.reshape(count, rows, width)
    main_pieces = [blocks[place]]
    pair_pieces = [blocks[(place + half) % count]]
    for d in range(1, count):
        target = (place + d) % count
        payload = jnp.concatenate([blocks[target], blocks[(target + half) % count]], axis=0)
        got = lax.ppermute(payload, "row", [(z, (z + d) % count) for z in range(count)])
        main_pieces.append(got[:rows])
        pair_pieces.append(got[rows:])

    def in_order(pieces):
        ordered = []
        for q in range(count):
            picked = pieces[0]
            for d in range(1, count):
                picked = jnp.where((place - d) % count == q, pieces[d], picked)
            ordered.append(picked)
        return jnp.concatenate(ordered, axis=1)

    rows_traj = product(in_order(main_pieces), terminal_states)
    pair_traj = product(in_order(pair_pieces), terminal_states)
    partial = jnp.sum(rows_traj * pair_traj, axis=0)
    cols = terminal_states.shape[1] // count
    total = lax.dynamic_slice_in_dim(partial, place * cols, cols, 0)
    if half == 2:
        partner = [(z, z ^ 1) for z in range(count)]
        sent = lax.dynamic_slice_in_dim(partial, (place ^ 1) * cols, cols, 0)
        total = total + lax.ppermute(sent, "row", partner)
    else:
        for e in range(1, half):
            target = (place + e) % count
            sent = lax.dynamic_slice_in_dim(partial, target * cols, cols, 0)
            total = total + lax.ppermute(sent, "row", [(z, (z + e) % count) for z in range(count)])
    section_cost = total / state_dim
    return (rows_traj[None], section_cost[None])


def solution(mesh):
    in_specs = (P("tm", "row", None), P("row", None), P())
    out_specs = (P("tm", "row", None), P("tm", "row"))
    return jax.shard_map(body, mesh=mesh, in_specs=in_specs, out_specs=out_specs, check_vma=False)
```

```python
import jax
import jax.numpy as jnp
from jax import lax
from jax.sharding import PartitionSpec as P

CHUNKS = 2


def product(left, right):
    return jnp.dot(left, right, precision=lax.Precision.HIGH, preferred_element_type=jnp.float32)


def line_gather(block, place, count):
    rightward = block
    leftward = block
    from_left = []
    from_right = []
    for t in range(1, count):
        rightward = lax.ppermute(rightward, "row", [(z, z + 1) for z in range(t - 1, count - 1)])
        leftward = lax.ppermute(leftward, "row", [(z, z - 1) for z in range(1, count - t + 1)])
        from_left.append(rightward)
        from_right.append(leftward)
    by_offset = jnp.concatenate(from_left[::-1] + [block] + from_right, axis=0)
    rows = block.shape[0]
    return lax.dynamic_slice_in_dim(by_offset, (count - 1 - place) * rows, count * rows, 0)


def body(section_maps, terminal_cost, terminal_states):
    groups = lax.axis_size("tm")
    count = lax.axis_size("row")
    group = lax.axis_index("tm")
    place = lax.axis_index("row")
    state_dim = terminal_cost.shape[1]
    width = state_dim // count

    local = section_maps[0]
    cut = local.shape[0] // 2
    upper = line_gather(local[:cut], place, count).reshape(count, cut, local.shape[1])
    lower = line_gather(local[cut:], place, count).reshape(count, cut, local.shape[1])
    whole_map = jnp.concatenate([upper, lower], axis=1).reshape(count * local.shape[0], local.shape[1])
    whole_map = lax.optimization_barrier(whole_map)
    rows_id = lax.broadcasted_iota(jnp.int32, (state_dim, width), 0)
    cols_id = lax.broadcasted_iota(jnp.int32, (state_dim, width), 1) + place * width
    identity_cols = (rows_id == cols_id).astype(jnp.float32)
    incoming = lax.optimization_barrier(jnp.concatenate([identity_cols, terminal_cost.T], axis=0))

    step = width // CHUNKS
    incoming = [incoming[:, j * step:(j + 1) * step] for j in range(CHUNKS)]
    own = [None] * CHUNKS
    for k in range(groups - 1, -1, -1):
        for j in range(CHUNKS):
            fresh = product(whole_map, incoming[j])
            own[j] = fresh if own[j] is None else jnp.where(group == k, fresh, own[j])
            if k > 0:
                got = lax.ppermute(fresh, "tm", [(k, k - 1)])
                incoming[j] = jnp.where(group == k - 1, got, incoming[j])

    own_cols = jnp.concatenate(own, axis=1)
    rows = own_cols.shape[0] // count
    half = count // 2
    blocks = own_cols.reshape(count, rows, width)
    main_pieces = [blocks[place]]
    pair_pieces = [blocks[(place + half) % count]]
    for d in range(1, count):
        target = (place + d) % count
        payload = jnp.concatenate([blocks[target], blocks[(target + half) % count]], axis=0)
        got = lax.ppermute(payload, "row", [(z, (z + d) % count) for z in range(count)])
        main_pieces.append(got[:rows])
        pair_pieces.append(got[rows:])

    def in_order(pieces):
        ordered = []
        for q in range(count):
            picked = pieces[0]
            for d in range(1, count):
                picked = jnp.where((place - d) % count == q, pieces[d], picked)
            ordered.append(picked)
        return jnp.concatenate(ordered, axis=1)

    rows_traj = product(in_order(main_pieces), terminal_states)
    pair_traj = product(in_order(pair_pieces), terminal_states)
    partial = jnp.sum(rows_traj * pair_traj, axis=0)
    cols = terminal_states.shape[1] // count
    total = lax.dynamic_slice_in_dim(partial, place * cols, cols, 0)
    if half == 2:
        partner = [(z, z ^ 1) for z in range(count)]
        sent = lax.dynamic_slice_in_dim(partial, (place ^ 1) * cols, cols, 0)
        total = total + lax.ppermute(sent, "row", partner)
    else:
        for e in range(1, half):
            target = (place + e) % count
            sent = lax.dynamic_slice_in_dim(partial, target * cols, cols, 0)
            total = total + lax.ppermute(sent, "row", [(z, (z + e) % count) for z in range(count)])
    section_cost = total / state_dim
    return (rows_traj[None], section_cost[None])


def solution(mesh):
    in_specs = (P("tm", "row", None), P("row", None), P())
    out_specs = (P("tm", "row", None), P("tm", "row"))
    return jax.shard_map(body, mesh=mesh, in_specs=in_specs, out_specs=out_specs, check_vma=False)
```

```python
import jax
import jax.numpy as jnp
from jax import lax
from jax.sharding import PartitionSpec as P

CHUNKS = 2


def product(left, right):
    return jnp.dot(left, right, precision=lax.Precision.HIGH, preferred_element_type=jnp.float32)


def line_gather(block, place, count):
    rightward = block
    leftward = block
    from_left = []
    from_right = []
    for t in range(1, count):
        rightward = lax.ppermute(rightward, "row", [(z, z + 1) for z in range(t - 1, count - 1)])
        leftward = lax.ppermute(leftward, "row", [(z, z - 1) for z in range(1, count - t + 1)])
        from_left.append(rightward)
        from_right.append(leftward)
    by_offset = jnp.concatenate(from_left[::-1] + [block] + from_right, axis=0)
    rows = block.shape[0]
    return lax.dynamic_slice_in_dim(by_offset, (count - 1 - place) * rows, count * rows, 0)


def body(section_maps, terminal_cost, terminal_states):
    groups = lax.axis_size("tm")
    count = lax.axis_size("row")
    group = lax.axis_index("tm")
    place = lax.axis_index("row")
    state_dim = terminal_cost.shape[1]
    width = state_dim // count

    local = section_maps[0]
    cut = local.shape[0] // 2
    upper = line_gather(local[:cut], place, count).reshape(count, cut, local.shape[1])
    lower = line_gather(local[cut:], place, count).reshape(count, cut, local.shape[1])
    whole_map = jnp.concatenate([upper, lower], axis=1).reshape(count * local.shape[0], local.shape[1])
    whole_map = lax.optimization_barrier(whole_map)
    rows_id = lax.broadcasted_iota(jnp.int32, (state_dim, width), 0)
    cols_id = lax.broadcasted_iota(jnp.int32, (state_dim, width), 1) + place * width
    identity_cols = (rows_id == cols_id).astype(jnp.float32)
    incoming = jnp.concatenate([identity_cols, terminal_cost.T], axis=0)

    step = width // CHUNKS
    incoming = [incoming[:, j * step:(j + 1) * step] for j in range(CHUNKS)]
    own = [None] * CHUNKS
    for k in range(groups - 1, -1, -1):
        for j in range(CHUNKS):
            fresh = product(whole_map, incoming[j])
            own[j] = fresh if own[j] is None else jnp.where(group == k, fresh, own[j])
            if k > 0:
                got = lax.ppermute(fresh, "tm", [(k, k - 1)])
                incoming[j] = jnp.where(group == k - 1, got, incoming[j])

    own_cols = jnp.concatenate(own, axis=1)
    rows = own_cols.shape[0] // count
    half = count // 2
    blocks = own_cols.reshape(count, rows, width)
    main_pieces = [blocks[place]]
    pair_pieces = [blocks[(place + half) % count]]
    for d in range(1, count):
        target = (place + d) % count
        payload = jnp.concatenate([blocks[target], blocks[(target + half) % count]], axis=0)
        got = lax.ppermute(payload, "row", [(z, (z + d) % count) for z in range(count)])
        main_pieces.append(got[:rows])
        pair_pieces.append(got[rows:])

    def in_order(pieces):
        ordered = []
        for q in range(count):
            picked = pieces[0]
            for d in range(1, count):
                picked = jnp.where((place - d) % count == q, pieces[d], picked)
            ordered.append(picked)
        return jnp.concatenate(ordered, axis=1)

    both_traj = product(jnp.concatenate([in_order(main_pieces), in_order(pair_pieces)], axis=0), terminal_states)
    rows_traj = both_traj[:rows]
    pair_traj = both_traj[rows:]
    partial = jnp.sum(rows_traj * pair_traj, axis=0)
    cols = terminal_states.shape[1] // count
    total = lax.dynamic_slice_in_dim(partial, place * cols, cols, 0)
    if half == 2:
        partner = [(z, z ^ 1) for z in range(count)]
        sent = lax.dynamic_slice_in_dim(partial, (place ^ 1) * cols, cols, 0)
        total = total + lax.ppermute(sent, "row", partner)
    else:
        for e in range(1, half):
            target = (place + e) % count
            sent = lax.dynamic_slice_in_dim(partial, target * cols, cols, 0)
            total = total + lax.ppermute(sent, "row", [(z, (z + e) % count) for z in range(count)])
    section_cost = total / state_dim
    return (rows_traj[None], section_cost[None])


def solution(mesh):
    in_specs = (P("tm", "row", None), P("row", None), P())
    out_specs = (P("tm", "row", None), P("tm", "row"))
    return jax.shard_map(body, mesh=mesh, in_specs=in_specs, out_specs=out_specs, check_vma=False)
```

```python
import jax
import jax.numpy as jnp
from jax import lax
from jax.sharding import PartitionSpec as P

CHUNKS = 2


def product(left, right):
    return jnp.dot(left, right, precision=lax.Precision.HIGH, preferred_element_type=jnp.float32)


def line_gather(block, place, count):
    rightward = block
    leftward = block
    from_left = []
    from_right = []
    for t in range(1, count):
        rightward = lax.ppermute(rightward, "row", [(z, z + 1) for z in range(t - 1, count - 1)])
        leftward = lax.ppermute(leftward, "row", [(z, z - 1) for z in range(1, count - t + 1)])
        from_left.append(rightward)
        from_right.append(leftward)
    by_offset = jnp.concatenate(from_left[::-1] + [block] + from_right, axis=0)
    rows = block.shape[0]
    return lax.dynamic_slice_in_dim(by_offset, (count - 1 - place) * rows, count * rows, 0)


def body(section_maps, terminal_cost, terminal_states):
    groups = lax.axis_size("tm")
    count = lax.axis_size("row")
    group = lax.axis_index("tm")
    place = lax.axis_index("row")
    state_dim = terminal_cost.shape[1]
    width = state_dim // count

    local = section_maps[0]
    cut = local.shape[0] // 2
    upper = line_gather(local[:cut], place, count).reshape(count, cut, local.shape[1])
    lower = line_gather(local[cut:], place, count).reshape(count, cut, local.shape[1])
    whole_map = jnp.concatenate([upper, lower], axis=1).reshape(count * local.shape[0], local.shape[1])
    whole_map = lax.optimization_barrier(whole_map)
    rows_id = lax.broadcasted_iota(jnp.int32, (state_dim, width), 0)
    cols_id = lax.broadcasted_iota(jnp.int32, (state_dim, width), 1) + place * width
    identity_cols = (rows_id == cols_id).astype(jnp.float32)
    incoming = jnp.concatenate([identity_cols, terminal_cost.T], axis=0)

    step = width // CHUNKS
    incoming = [incoming[:, j * step:(j + 1) * step] for j in range(CHUNKS)]
    own = [None] * CHUNKS
    for k in range(groups - 1, -1, -1):
        for j in range(CHUNKS):
            fresh = product(whole_map, incoming[j])
            own[j] = fresh if own[j] is None else jnp.where(group == k, fresh, own[j])
            if k > 0:
                got = lax.ppermute(fresh, "tm", [(k, k - 1)])
                incoming[j] = jnp.where(group == k - 1, got, incoming[j])

    own_cols = jnp.concatenate(own, axis=1)
    rows = own_cols.shape[0] // count
    half = count // 2
    blocks = own_cols.reshape(count, rows, width)
    def states_of(source):
        return lax.dynamic_slice_in_dim(terminal_states, source * width, width, 0)

    own_both = jnp.concatenate([blocks[place], blocks[(place + half) % count]], axis=0)
    both_traj = product(own_both, states_of(place))
    for d in range(1, count):
        target = (place + d) % count
        payload = jnp.concatenate([blocks[target], blocks[(target + half) % count]], axis=0)
        got = lax.ppermute(payload, "row", [(z, (z + d) % count) for z in range(count)])
        both_traj = both_traj + product(got, states_of((place - d) % count))
    rows_traj = both_traj[:rows]
    pair_traj = both_traj[rows:]
    partial = jnp.sum(rows_traj * pair_traj, axis=0)
    cols = terminal_states.shape[1] // count
    total = lax.dynamic_slice_in_dim(partial, place * cols, cols, 0)
    if half == 2:
        partner = [(z, z ^ 1) for z in range(count)]
        sent = lax.dynamic_slice_in_dim(partial, (place ^ 1) * cols, cols, 0)
        total = total + lax.ppermute(sent, "row", partner)
    else:
        for e in range(1, half):
            target = (place + e) % count
            sent = lax.dynamic_slice_in_dim(partial, target * cols, cols, 0)
            total = total + lax.ppermute(sent, "row", [(z, (z + e) % count) for z in range(count)])
    section_cost = total / state_dim
    return (rows_traj[None], section_cost[None])


def solution(mesh):
    in_specs = (P("tm", "row", None), P("row", None), P())
    out_specs = (P("tm", "row", None), P("tm", "row"))
    return jax.shard_map(body, mesh=mesh, in_specs=in_specs, out_specs=out_specs, check_vma=False)
```

```python
import jax
import jax.numpy as jnp
from jax import lax
from jax.sharding import PartitionSpec as P

CHUNKS = 2


def product(left, right):
    return jnp.dot(left, right, precision=lax.Precision.HIGH, preferred_element_type=jnp.float32)


def line_gather(block, place, count):
    rightward = block
    leftward = block
    from_left = []
    from_right = []
    for t in range(1, count):
        rightward = lax.ppermute(rightward, "row", [(z, z + 1) for z in range(t - 1, count - 1)])
        leftward = lax.ppermute(leftward, "row", [(z, z - 1) for z in range(1, count - t + 1)])
        from_left.append(rightward)
        from_right.append(leftward)
    by_offset = jnp.concatenate(from_left[::-1] + [block] + from_right, axis=0)
    rows = block.shape[0]
    return lax.dynamic_slice_in_dim(by_offset, (count - 1 - place) * rows, count * rows, 0)


def body(section_maps, terminal_cost, terminal_states):
    groups = lax.axis_size("tm")
    count = lax.axis_size("row")
    group = lax.axis_index("tm")
    place = lax.axis_index("row")
    state_dim = terminal_cost.shape[1]
    width = state_dim // count

    local = section_maps[0]
    cut = local.shape[0] // 2
    upper = line_gather(local[:cut], place, count).reshape(count, cut, local.shape[1])
    lower = line_gather(local[cut:], place, count).reshape(count, cut, local.shape[1])
    whole_map = jnp.concatenate([upper, lower], axis=1).reshape(count * local.shape[0], local.shape[1])
    whole_map = lax.optimization_barrier(whole_map)
    rows_id = lax.broadcasted_iota(jnp.int32, (state_dim, width), 0)
    cols_id = lax.broadcasted_iota(jnp.int32, (state_dim, width), 1) + place * width
    identity_cols = (rows_id == cols_id).astype(jnp.float32)
    incoming = jnp.concatenate([identity_cols, terminal_cost.T], axis=0)

    step = width // CHUNKS
    incoming = [incoming[:, j * step:(j + 1) * step] for j in range(CHUNKS)]
    own = [None] * CHUNKS
    for k in range(groups - 1, -1, -1):
        for j in range(CHUNKS):
            if k == groups - 1:
                picked = lax.dynamic_slice_in_dim(whole_map, place * width + j * step, step, 1)
                fresh = picked + product(whole_map[:, state_dim:], incoming[j][state_dim:])
            else:
                fresh = product(whole_map, incoming[j])
            own[j] = fresh if own[j] is None else jnp.where(group == k, fresh, own[j])
            if k > 0:
                got = lax.ppermute(fresh, "tm", [(k, k - 1)])
                incoming[j] = jnp.where(group == k - 1, got, incoming[j])

    own_cols = jnp.concatenate(own, axis=1)
    rows = own_cols.shape[0] // count
    half = count // 2
    blocks = own_cols.reshape(count, rows, width)
    main_pieces = [blocks[place]]
    pair_pieces = [blocks[(place + half) % count]]
    for d in range(1, count):
        target = (place + d) % count
        payload = jnp.concatenate([blocks[target], blocks[(target + half) % count]], axis=0)
        got = lax.ppermute(payload, "row", [(z, (z + d) % count) for z in range(count)])
        main_pieces.append(got[:rows])
        pair_pieces.append(got[rows:])

    def in_order(pieces):
        ordered = []
        for q in range(count):
            picked = pieces[0]
            for d in range(1, count):
                picked = jnp.where((place - d) % count == q, pieces[d], picked)
            ordered.append(picked)
        return jnp.concatenate(ordered, axis=1)

    rows_traj = product(in_order(main_pieces), terminal_states)
    pair_traj = product(in_order(pair_pieces), terminal_states)
    partial = jnp.sum(rows_traj * pair_traj, axis=0)
    cols = terminal_states.shape[1] // count
    total = lax.dynamic_slice_in_dim(partial, place * cols, cols, 0)
    if half == 2:
        partner = [(z, z ^ 1) for z in range(count)]
        sent = lax.dynamic_slice_in_dim(partial, (place ^ 1) * cols, cols, 0)
        total = total + lax.ppermute(sent, "row", partner)
    else:
        for e in range(1, half):
            target = (place + e) % count
            sent = lax.dynamic_slice_in_dim(partial, target * cols, cols, 0)
            total = total + lax.ppermute(sent, "row", [(z, (z + e) % count) for z in range(count)])
    section_cost = total / state_dim
    return (rows_traj[None], section_cost[None])


def solution(mesh):
    in_specs = (P("tm", "row", None), P("row", None), P())
    out_specs = (P("tm", "row", None), P("tm", "row"))
    return jax.shard_map(body, mesh=mesh, in_specs=in_specs, out_specs=out_specs, check_vma=False)
```

```python
import jax
import jax.numpy as jnp
from jax import lax
from jax.sharding import PartitionSpec as P

CHUNKS = 2


def product(left, right):
    return jnp.dot(left, right, precision=lax.Precision.HIGH, preferred_element_type=jnp.float32)


def line_gather(block, place, count):
    rightward = block
    leftward = block
    from_left = []
    from_right = []
    for t in range(1, count):
        rightward = lax.ppermute(rightward, "row", [(z, z + 1) for z in range(t - 1, count - 1)])
        leftward = lax.ppermute(leftward, "row", [(z, z - 1) for z in range(1, count - t + 1)])
        from_left.append(rightward)
        from_right.append(leftward)
    by_offset = jnp.concatenate(from_left[::-1] + [block] + from_right, axis=0)
    rows = block.shape[0]
    return lax.dynamic_slice_in_dim(by_offset, (count - 1 - place) * rows, count * rows, 0)


def body(section_maps, terminal_cost, terminal_states):
    groups = lax.axis_size("tm")
    count = lax.axis_size("row")
    group = lax.axis_index("tm")
    place = lax.axis_index("row")
    state_dim = terminal_cost.shape[1]
    width = state_dim // count

    local = section_maps[0]
    cut = local.shape[0] // 2
    upper = line_gather(local[:cut], place, count).reshape(count, cut, local.shape[1])
    lower = line_gather(local[cut:], place, count).reshape(count, cut, local.shape[1])
    whole_map = jnp.concatenate([upper, lower], axis=1).reshape(count * local.shape[0], local.shape[1])
    whole_map = lax.optimization_barrier(whole_map)
    rows_id = lax.broadcasted_iota(jnp.int32, (state_dim, width), 0)
    cols_id = lax.broadcasted_iota(jnp.int32, (state_dim, width), 1) + place * width
    identity_cols = (rows_id == cols_id).astype(jnp.float32)
    incoming = jnp.concatenate([identity_cols, terminal_cost.T], axis=0)

    step = width // CHUNKS
    incoming = [incoming[:, j * step:(j + 1) * step] for j in range(CHUNKS)]
    own = [None] * CHUNKS
    for k in range(groups - 1, -1, -1):
        for j in range(CHUNKS):
            fresh = product(whole_map, incoming[j])
            own[j] = fresh if own[j] is None else jnp.where(group == k, fresh, own[j])
            if k > 0:
                incoming[j] = lax.ppermute(fresh, "tm", [(k, k - 1)])

    own_cols = jnp.concatenate(own, axis=1)
    rows = own_cols.shape[0] // count
    half = count // 2
    blocks = own_cols.reshape(count, rows, width)
    main_pieces = [blocks[place]]
    pair_pieces = [blocks[(place + half) % count]]
    for d in range(1, count):
        target = (place + d) % count
        payload = jnp.concatenate([blocks[target], blocks[(target + half) % count]], axis=0)
        got = lax.ppermute(payload, "row", [(z, (z + d) % count) for z in range(count)])
        main_pieces.append(got[:rows])
        pair_pieces.append(got[rows:])

    def in_order(pieces):
        ordered = []
        for q in range(count):
            picked = pieces[0]
            for d in range(1, count):
                picked = jnp.where((place - d) % count == q, pieces[d], picked)
            ordered.append(picked)
        return jnp.concatenate(ordered, axis=1)

    rows_traj = product(in_order(main_pieces), terminal_states)
    pair_traj = product(in_order(pair_pieces), terminal_states)
    partial = jnp.sum(rows_traj * pair_traj, axis=0)
    cols = terminal_states.shape[1] // count
    total = lax.dynamic_slice_in_dim(partial, place * cols, cols, 0)
    if half == 2:
        partner = [(z, z ^ 1) for z in range(count)]
        sent = lax.dynamic_slice_in_dim(partial, (place ^ 1) * cols, cols, 0)
        total = total + lax.ppermute(sent, "row", partner)
    else:
        for e in range(1, half):
            target = (place + e) % count
            sent = lax.dynamic_slice_in_dim(partial, target * cols, cols, 0)
            total = total + lax.ppermute(sent, "row", [(z, (z + e) % count) for z in range(count)])
    section_cost = total / state_dim
    return (rows_traj[None], section_cost[None])


def solution(mesh):
    in_specs = (P("tm", "row", None), P("row", None), P())
    out_specs = (P("tm", "row", None), P("tm", "row"))
    return jax.shard_map(body, mesh=mesh, in_specs=in_specs, out_specs=out_specs, check_vma=False)
```

```python
import jax
import jax.numpy as jnp
from jax import lax
from jax.sharding import PartitionSpec as P

CHUNKS = 4


def product(left, right):
    return jnp.dot(left, right, precision=lax.Precision.HIGH, preferred_element_type=jnp.float32)


def line_gather(block, place, count):
    rightward = block
    leftward = block
    from_left = []
    from_right = []
    for t in range(1, count):
        rightward = lax.ppermute(rightward, "row", [(z, z + 1) for z in range(t - 1, count - 1)])
        leftward = lax.ppermute(leftward, "row", [(z, z - 1) for z in range(1, count - t + 1)])
        from_left.append(rightward)
        from_right.append(leftward)
    by_offset = jnp.concatenate(from_left[::-1] + [block] + from_right, axis=0)
    rows = block.shape[0]
    return lax.dynamic_slice_in_dim(by_offset, (count - 1 - place) * rows, count * rows, 0)


def body(section_maps, terminal_cost, terminal_states):
    groups = lax.axis_size("tm")
    count = lax.axis_size("row")
    group = lax.axis_index("tm")
    place = lax.axis_index("row")
    state_dim = terminal_cost.shape[1]
    width = state_dim // count

    local = section_maps[0]
    cut = local.shape[0] // 2
    upper = line_gather(local[:cut], place, count).reshape(count, cut, local.shape[1])
    lower = line_gather(local[cut:], place, count).reshape(count, cut, local.shape[1])
    whole_map = jnp.concatenate([upper, lower], axis=1).reshape(count * local.shape[0], local.shape[1])
    whole_map = lax.optimization_barrier(whole_map)
    rows_id = lax.broadcasted_iota(jnp.int32, (state_dim, width), 0)
    cols_id = lax.broadcasted_iota(jnp.int32, (state_dim, width), 1) + place * width
    identity_cols = (rows_id == cols_id).astype(jnp.float32)
    incoming = jnp.concatenate([identity_cols, terminal_cost.T], axis=0)

    step = width // CHUNKS
    incoming = [incoming[:, j * step:(j + 1) * step] for j in range(CHUNKS)]
    own = [None] * CHUNKS
    for k in range(groups - 1, -1, -1):
        for j in range(CHUNKS):
            fresh = product(whole_map, incoming[j])
            own[j] = fresh if own[j] is None else jnp.where(group == k, fresh, own[j])
            if k > 0:
                incoming[j] = lax.ppermute(fresh, "tm", [(k, k - 1)])

    own_cols = jnp.concatenate(own, axis=1)
    rows = own_cols.shape[0] // count
    half = count // 2
    blocks = own_cols.reshape(count, rows, width)
    main_pieces = [blocks[place]]
    pair_pieces = [blocks[(place + half) % count]]
    for d in range(1, count):
        target = (place + d) % count
        payload = jnp.concatenate([blocks[target], blocks[(target + half) % count]], axis=0)
        got = lax.ppermute(payload, "row", [(z, (z + d) % count) for z in range(count)])
        main_pieces.append(got[:rows])
        pair_pieces.append(got[rows:])

    def in_order(pieces):
        ordered = []
        for q in range(count):
            picked = pieces[0]
            for d in range(1, count):
                picked = jnp.where((place - d) % count == q, pieces[d], picked)
            ordered.append(picked)
        return jnp.concatenate(ordered, axis=1)

    rows_traj = product(in_order(main_pieces), terminal_states)
    pair_traj = product(in_order(pair_pieces), terminal_states)
    partial = jnp.sum(rows_traj * pair_traj, axis=0)
    cols = terminal_states.shape[1] // count
    total = lax.dynamic_slice_in_dim(partial, place * cols, cols, 0)
    if half == 2:
        partner = [(z, z ^ 1) for z in range(count)]
        sent = lax.dynamic_slice_in_dim(partial, (place ^ 1) * cols, cols, 0)
        total = total + lax.ppermute(sent, "row", partner)
    else:
        for e in range(1, half):
            target = (place + e) % count
            sent = lax.dynamic_slice_in_dim(partial, target * cols, cols, 0)
            total = total + lax.ppermute(sent, "row", [(z, (z + e) % count) for z in range(count)])
    section_cost = total / state_dim
    return (rows_traj[None], section_cost[None])


def solution(mesh):
    in_specs = (P("tm", "row", None), P("row", None), P())
    out_specs = (P("tm", "row", None), P("tm", "row"))
    return jax.shard_map(body, mesh=mesh, in_specs=in_specs, out_specs=out_specs, check_vma=False)
```

```python
import jax
import jax.numpy as jnp
from jax import lax
from jax.sharding import PartitionSpec as P

CHUNKS = 2


def product(left, right):
    return jnp.dot(left, right, precision=lax.Precision.HIGH, preferred_element_type=jnp.float32)


def line_gather(block, place, count):
    rightward = block
    leftward = block
    from_left = []
    from_right = []
    for t in range(1, count):
        rightward = lax.ppermute(rightward, "row", [(z, z + 1) for z in range(t - 1, count - 1)])
        leftward = lax.ppermute(leftward, "row", [(z, z - 1) for z in range(1, count - t + 1)])
        from_left.append(rightward)
        from_right.append(leftward)
    by_offset = jnp.concatenate(from_left[::-1] + [block] + from_right, axis=0)
    rows = block.shape[0]
    return lax.dynamic_slice_in_dim(by_offset, (count - 1 - place) * rows, count * rows, 0)


def body(section_maps, terminal_cost, terminal_states):
    groups = lax.axis_size("tm")
    count = lax.axis_size("row")
    group = lax.axis_index("tm")
    place = lax.axis_index("row")
    state_dim = terminal_cost.shape[1]
    width = state_dim // count

    local = section_maps[0]
    cut = local.shape[0] // 2
    upper = line_gather(local[:cut], place, count).reshape(count, cut, local.shape[1])
    lower = line_gather(local[cut:], place, count).reshape(count, cut, local.shape[1])
    whole_map = jnp.concatenate([upper, lower], axis=1).reshape(count * local.shape[0], local.shape[1])
    whole_map = lax.optimization_barrier(whole_map)
    rows_id = lax.broadcasted_iota(jnp.int32, (state_dim, width), 0)
    cols_id = lax.broadcasted_iota(jnp.int32, (state_dim, width), 1) + place * width
    identity_cols = (rows_id == cols_id).astype(jnp.float32)
    incoming = jnp.concatenate([identity_cols, terminal_cost.T], axis=0)

    step = width // CHUNKS
    incoming = [incoming[:, j * step:(j + 1) * step] for j in range(CHUNKS)]
    own = [None] * CHUNKS
    for k in range(groups - 1, -1, -1):
        for j in range(CHUNKS):
            fresh = product(whole_map, incoming[j])
            own[j] = fresh if own[j] is None else jnp.where(group == k, fresh, own[j])
            if k > 0:
                incoming[j] = lax.ppermute(fresh, "tm", [(k, k - 1)])

    own_cols = jnp.concatenate(own, axis=1)
    rows = own_cols.shape[0] // count
    half = count // 2
    blocks = own_cols.reshape(count, rows, width)
    main_pieces = [blocks[place]]
    pair_pieces = [blocks[(place + half) % count]]
    for d in range(1, count):
        target = (place + d) % count
        payload = jnp.concatenate([blocks[target], blocks[(target + half) % count]], axis=0)
        got = lax.ppermute(payload, "row", [(z, (z + d) % count) for z in range(count)])
        main_pieces.append(got[:rows])
        pair_pieces.append(got[rows:])

    def in_order(pieces):
        by_offset = jnp.concatenate(pieces[::-1] + pieces[:0:-1], axis=1)
        return lax.dynamic_slice_in_dim(by_offset, (count - 1 - place) * width, count * width, 1)

    rows_traj = product(in_order(main_pieces), terminal_states)
    pair_traj = product(in_order(pair_pieces), terminal_states)
    partial = jnp.sum(rows_traj * pair_traj, axis=0)
    cols = terminal_states.shape[1] // count
    total = lax.dynamic_slice_in_dim(partial, place * cols, cols, 0)
    if half == 2:
        partner = [(z, z ^ 1) for z in range(count)]
        sent = lax.dynamic_slice_in_dim(partial, (place ^ 1) * cols, cols, 0)
        total = total + lax.ppermute(sent, "row", partner)
    else:
        for e in range(1, half):
            target = (place + e) % count
            sent = lax.dynamic_slice_in_dim(partial, target * cols, cols, 0)
            total = total + lax.ppermute(sent, "row", [(z, (z + e) % count) for z in range(count)])
    section_cost = total / state_dim
    return (rows_traj[None], section_cost[None])


def solution(mesh):
    in_specs = (P("tm", "row", None), P("row", None), P())
    out_specs = (P("tm", "row", None), P("tm", "row"))
    return jax.shard_map(body, mesh=mesh, in_specs=in_specs, out_specs=out_specs, check_vma=False)
```

```python
import jax
import jax.numpy as jnp
from jax import lax
from jax.sharding import PartitionSpec as P

CHUNKS = 2


def product(left, right):
    return jnp.dot(left, right, precision=lax.Precision.HIGH, preferred_element_type=jnp.float32)


def line_gather(block, place, count):
    rightward = block
    leftward = block
    from_left = []
    from_right = []
    for t in range(1, count):
        rightward = lax.ppermute(rightward, "row", [(z, z + 1) for z in range(t - 1, count - 1)])
        leftward = lax.ppermute(leftward, "row", [(z, z - 1) for z in range(1, count - t + 1)])
        from_left.append(rightward)
        from_right.append(leftward)
    by_offset = jnp.concatenate(from_left[::-1] + [block] + from_right, axis=0)
    rows = block.shape[0]
    return lax.dynamic_slice_in_dim(by_offset, (count - 1 - place) * rows, count * rows, 0)


def body(section_maps, terminal_cost, terminal_states):
    groups = lax.axis_size("tm")
    count = lax.axis_size("row")
    group = lax.axis_index("tm")
    place = lax.axis_index("row")
    state_dim = terminal_cost.shape[1]
    width = state_dim // count

    local = section_maps[0]
    cut = local.shape[0] // 2
    upper = line_gather(local[:cut], place, count).reshape(count, cut, local.shape[1])
    lower = line_gather(local[cut:], place, count).reshape(count, cut, local.shape[1])
    whole_map = jnp.concatenate([upper, lower], axis=1).reshape(count * local.shape[0], local.shape[1])
    whole_map = lax.optimization_barrier(whole_map)
    rows_id = lax.broadcasted_iota(jnp.int32, (state_dim, width), 0)
    cols_id = lax.broadcasted_iota(jnp.int32, (state_dim, width), 1) + place * width
    identity_cols = (rows_id == cols_id).astype(jnp.float32)
    incoming = jnp.concatenate([identity_cols, terminal_cost.T], axis=0)

    step = width // CHUNKS
    incoming = [incoming[:, j * step:(j + 1) * step] for j in range(CHUNKS)]
    own = [None] * CHUNKS
    for k in range(groups - 1, -1, -1):
        for j in range(CHUNKS):
            fresh = product(whole_map, incoming[j])
            own[j] = fresh if own[j] is None else jnp.where(group == k, fresh, own[j])
            if k > 0:
                incoming[j] = lax.ppermute(fresh, "tm", [(k, k - 1)])

    own_cols = jnp.concatenate(own, axis=1)
    rows = own_cols.shape[0] // count
    half = count // 2
    blocks = own_cols.reshape(count, rows, width)
    pieces = [jnp.concatenate([blocks[place], blocks[(place + half) % count]], axis=0)]
    for d in range(1, count):
        target = (place + d) % count
        payload = jnp.concatenate([blocks[target], blocks[(target + half) % count]], axis=0)
        pieces.append(lax.ppermute(payload, "row", [(z, (z + d) % count) for z in range(count)]))

    def in_order(pieces):
        by_offset = jnp.concatenate(pieces[::-1] + pieces[:0:-1], axis=1)
        return lax.dynamic_slice_in_dim(by_offset, (count - 1 - place) * width, count * width, 1)

    both_traj = product(in_order(pieces), terminal_states)
    rows_traj = both_traj[:rows]
    pair_traj = both_traj[rows:]
    partial = jnp.sum(rows_traj * pair_traj, axis=0)
    cols = terminal_states.shape[1] // count
    total = lax.dynamic_slice_in_dim(partial, place * cols, cols, 0)
    if half == 2:
        partner = [(z, z ^ 1) for z in range(count)]
        sent = lax.dynamic_slice_in_dim(partial, (place ^ 1) * cols, cols, 0)
        total = total + lax.ppermute(sent, "row", partner)
    else:
        for e in range(1, half):
            target = (place + e) % count
            sent = lax.dynamic_slice_in_dim(partial, target * cols, cols, 0)
            total = total + lax.ppermute(sent, "row", [(z, (z + e) % count) for z in range(count)])
    section_cost = total / state_dim
    return (rows_traj[None], section_cost[None])


def solution(mesh):
    in_specs = (P("tm", "row", None), P("row", None), P())
    out_specs = (P("tm", "row", None), P("tm", "row"))
    return jax.shard_map(body, mesh=mesh, in_specs=in_specs, out_specs=out_specs, check_vma=False)
```

```python
import jax
import jax.numpy as jnp
from jax import lax
from jax.sharding import PartitionSpec as P

CHUNKS = 2


def product(left, right):
    return jnp.dot(left, right, precision=lax.Precision.HIGH, preferred_element_type=jnp.float32)


def line_gather(block, place, count):
    rightward = block
    leftward = block
    from_left = []
    from_right = []
    for t in range(1, count):
        rightward = lax.ppermute(rightward, "row", [(z, z + 1) for z in range(t - 1, count - 1)])
        leftward = lax.ppermute(leftward, "row", [(z, z - 1) for z in range(1, count - t + 1)])
        from_left.append(rightward)
        from_right.append(leftward)
    by_offset = jnp.concatenate(from_left[::-1] + [block] + from_right, axis=0)
    rows = block.shape[0]
    return lax.dynamic_slice_in_dim(by_offset, (count - 1 - place) * rows, count * rows, 0)


def body(section_maps, terminal_cost, terminal_states):
    groups = lax.axis_size("tm")
    count = lax.axis_size("row")
    group = lax.axis_index("tm")
    place = lax.axis_index("row")
    state_dim = terminal_cost.shape[1]
    width = state_dim // count

    local = section_maps[0]
    cut = local.shape[0] // 2
    upper = line_gather(local[:cut], place, count).reshape(count, cut, local.shape[1])
    lower = line_gather(local[cut:], place, count).reshape(count, cut, local.shape[1])
    whole_map = jnp.concatenate([upper, lower], axis=1).reshape(count * local.shape[0], local.shape[1])
    whole_map = lax.optimization_barrier(whole_map)
    rows_id = lax.broadcasted_iota(jnp.int32, (state_dim, width), 0)
    cols_id = lax.broadcasted_iota(jnp.int32, (state_dim, width), 1) + place * width
    identity_cols = (rows_id == cols_id).astype(jnp.float32)
    incoming = jnp.concatenate([identity_cols, terminal_cost.T], axis=0)

    step = width // CHUNKS
    incoming = [incoming[:, j * step:(j + 1) * step] for j in range(CHUNKS)]
    own = [None] * CHUNKS
    for k in range(groups - 1, -1, -1):
        for j in range(CHUNKS):
            if k == groups - 1:
                picked = lax.dynamic_slice_in_dim(whole_map, place * width + j * step, step, 1)
                fresh = picked + product(whole_map[:, state_dim:], incoming[j][state_dim:])
            else:
                fresh = product(whole_map, incoming[j])
            own[j] = fresh if own[j] is None else jnp.where(group == k, fresh, own[j])
            if k > 0:
                incoming[j] = lax.ppermute(fresh, "tm", [(k, k - 1)])

    own_cols = jnp.concatenate(own, axis=1)
    rows = own_cols.shape[0] // count
    half = count // 2
    blocks = own_cols.reshape(count, rows, width)
    main_pieces = [blocks[place]]
    pair_pieces = [blocks[(place + half) % count]]
    for d in range(1, count):
        target = (place + d) % count
        payload = jnp.concatenate([blocks[target], blocks[(target + half) % count]], axis=0)
        got = lax.ppermute(payload, "row", [(z, (z + d) % count) for z in range(count)])
        main_pieces.append(got[:rows])
        pair_pieces.append(got[rows:])

    def in_order(pieces):
        by_offset = jnp.concatenate(pieces[::-1] + pieces[:0:-1], axis=1)
        return lax.dynamic_slice_in_dim(by_offset, (count - 1 - place) * width, count * width, 1)

    rows_traj = product(in_order(main_pieces), terminal_states)
    pair_traj = product(in_order(pair_pieces), terminal_states)
    partial = jnp.sum(rows_traj * pair_traj, axis=0)
    cols = terminal_states.shape[1] // count
    total = lax.dynamic_slice_in_dim(partial, place * cols, cols, 0)
    if half == 2:
        partner = [(z, z ^ 1) for z in range(count)]
        sent = lax.dynamic_slice_in_dim(partial, (place ^ 1) * cols, cols, 0)
        total = total + lax.ppermute(sent, "row", partner)
    else:
        for e in range(1, half):
            target = (place + e) % count
            sent = lax.dynamic_slice_in_dim(partial, target * cols, cols, 0)
            total = total + lax.ppermute(sent, "row", [(z, (z + e) % count) for z in range(count)])
    section_cost = total / state_dim
    return (rows_traj[None], section_cost[None])


def solution(mesh):
    in_specs = (P("tm", "row", None), P("row", None), P())
    out_specs = (P("tm", "row", None), P("tm", "row"))
    return jax.shard_map(body, mesh=mesh, in_specs=in_specs, out_specs=out_specs, check_vma=False)
```
